128 devices in a mesh: row: 64 (over y, x, z_lo, core), col: 2 (over z_hi).
Axes of the slice: x: 4, y: 4, z: 4 (z_hi: 2, z_lo: 2; z = z_hi * 2 + z_lo), core: 2. Of those that a mesh axis runs over, the one named last changes fastest.
Arguments:
- dist_first: bfloat16 [32768, 32768], P('row', 'col'), may hold values from -0.34 to 0.34
- coupling: bfloat16 [32768, 256], P('row', 'col'), may hold values from 0.099609375 to 1
- dist_second: bfloat16 [256, 512], P(None, 'col'), may hold values from -12 to 12
- row_potential: float32 [32768], P('row'), may hold values from -150 to 120
- column_cost: float32 [512], P('col'), may hold values from -300 to 20
- column_mass: float32 [512], P('col'), may hold values from 0.5 to 2
Outputs:
- transport: bfloat16 [32768, 512], P('row', 'col')
- potential: float32 [512], P('col')
The draws below stay inside these ranges and needn't reach their ends.
All inputs are finite; a program needn't handle non-finite values.
Results may differ from the reference program's by a relative error of at most 0.0051.
Values may be sent and summed in bfloat16 or wider, within the bound.
No kernel may reach another device: no remote copies, remote signals or barrier semaphores. Data moves between devices by JAX's collectives and lax.ppermute only.
A program may use at most 128 MiB of HBM per device.

```python
import math
import jax
import jax.numpy as jnp

N = 32768
Q = 512
K = 256


def draw_dist_first(key, part):
    noise_key = jax.random.fold_in(jax.random.fold_in(key, 11), 0)
    values = jax.random.truncated_normal(noise_key, -6.0, 6.0, (N, N), jnp.float32) / math.sqrt(N)
    return jnp.clip(values, -0.34, 0.34).astype(jnp.bfloat16)


def draw_dist_second(key, part):
    noise_key = jax.random.fold_in(jax.random.fold_in(key, 53), 0)
    values = jax.random.truncated_normal(noise_key, -6.0, 6.0, (K, Q), jnp.float32) / math.sqrt(4.0 * K)
    return jnp.clip(values, -12.0, 12.0).astype(jnp.bfloat16)


def draw_row_potential(key, part):
    noise_key = jax.random.fold_in(jax.random.fold_in(key, 23), 0)
    ramp = jnp.arange(N, dtype=jnp.float32) / N
    values = 0.5 * jax.random.normal(noise_key, (N,), jnp.float32) + 1.2 * ramp
    return values


def draw_column_cost(key, part):
    noise_key = jax.random.fold_in(jax.random.fold_in(key, 37), 0)
    values = 0.5 * jax.random.truncated_normal(noise_key, -6.0, 6.0, (Q,), jnp.float32)
    return values


def level_of(key, extent, cuts, smallest, top_value):
    level = 1.0
    for axis_at, blocks in cuts:
        steps = jax.random.uniform(jax.random.fold_in(jax.random.fold_in(key, 6), axis_at), (blocks,), jnp.float32, smallest / len(cuts), top_value / len(cuts))
        level = level * jnp.repeat(jnp.exp(steps), extent[axis_at] // blocks).reshape((-1,) + (1,) * (len(extent) - 1 - axis_at))
    return level


def setup_inputs(seed: int = 0) -> dict:
    arg_keys = jax.random.split(jax.random.key(seed), 7)
    return {
        "dist_first": draw_dist_first(jax.random.fold_in(arg_keys[6], 71), 0),
        "coupling": jnp.clip(jnp.exp(math.log(1.0) - 2.306499 * jax.random.uniform(arg_keys[1], (N, K), jnp.float32) ** level_of(arg_keys[1], (N, K), ((0, 64), (1, 2)), -0.2, 0.2)), 0.099609375, 1.0).astype(jnp.bfloat16),
        "dist_second": draw_dist_second(jax.random.fold_in(arg_keys[6], 71), 0),
        "row_potential": draw_row_potential(jax.random.fold_in(arg_keys[6], 71), 0),
        "column_cost": draw_column_cost(jax.random.fold_in(arg_keys[6], 71), 0),
        "column_mass": jnp.clip(jnp.exp(math.log(2.0) - 1.3862944 * jax.random.uniform(arg_keys[5], (Q,), jnp.float32) ** level_of(arg_keys[5], (Q,), ((0, 2),), -0.2, 0.2)), 0.5, 2.0),
    }


def reference(dist_first, coupling, dist_second, row_potential, column_cost, column_mass):
    product = jnp.dot(coupling, dist_second, preferred_element_type=jnp.float32).astype(jnp.bfloat16)
    gradient = jnp.dot(dist_first, product, preferred_element_type=jnp.float32)
    scores = row_potential[:, None] + 2.0 * gradient - column_cost[None, :]
    highest = jnp.max(scores, axis=0)
    weights = jnp.exp(scores - highest[None, :])
    column_sum = jnp.sum(weights, axis=0)
    potential = jnp.log(column_mass) - highest - jnp.log(column_sum)
    transport = (weights * (N * column_mass / column_sum)[None, :]).astype(jnp.bfloat16)
    return transport, potential
```

```python
import jax
import jax.numpy as jnp
import numpy as np
from jax import lax
from jax.sharding import Mesh
from jax.sharding import PartitionSpec as P

N = 32768
AXES = ("yh", "yl", "x", "zl", "core", "zh")
ROWS = ("yh", "yl", "x", "zl", "core")
GATHER = ("yl", "x", "zl", "core")


def body(dist_first, coupling, dist_second, row_potential, column_cost, column_mass):
    zh = lax.axis_index("zh")
    yh = lax.axis_index("yh")
    blocks = coupling.shape[0]
    k_half = coupling.shape[1]
    q_half = dist_second.shape[1]

    coupling_x = lax.ppermute(coupling, "zh", [(0, 1), (1, 0)])
    second_x = lax.ppermute(dist_second, "zh", [(0, 1), (1, 0)])

    piece = jnp.concatenate([coupling, coupling_x], axis=1)
    into_other_half = [(0, 4), (2, 6), (5, 1), (7, 3)]
    moved = lax.ppermute(piece, ("yh", "yl", "zh"), into_other_half)
    piece = jnp.where(yh == zh, piece, moved)

    gathered = lax.all_gather(piece, GATHER, axis=0, tiled=True)

    second_full = jnp.concatenate([dist_second, second_x], axis=1)
    second_k = jnp.concatenate(
        [
            lax.dynamic_slice_in_dim(second_full, zh * k_half, k_half, axis=0),
            lax.dynamic_slice_in_dim(second_full, (1 - zh) * k_half, k_half, axis=0),
        ]
    )

    def partial_gradient(cols):
        product = jnp.dot(
            gathered, second_k[:, cols], preferred_element_type=jnp.float32
        ).astype(jnp.bfloat16)
        return jnp.dot(dist_first, product, preferred_element_type=jnp.float32)

    other_part = partial_gradient(slice(q_half, 2 * q_half))
    arrived = lax.ppermute(other_part, "zh", [(0, 1), (1, 0)])
    own_part = partial_gradient(slice(0, q_half))
    own_part, arrived = lax.optimization_barrier((own_part, arrived))
    gradient = own_part + arrived

    scores = row_potential[:, None] + 2.0 * gradient - column_cost[None, :]
    local_high = jnp.max(scores, axis=0)
    local_sum = jnp.sum(jnp.exp(scores - local_high[None, :]), axis=0)
    stats = lax.all_gather(jnp.stack([local_high, local_sum]), ROWS, axis=0, tiled=False)
    highest = jnp.max(stats[:, 0], axis=0)
    column_sum = jnp.sum(stats[:, 1] * jnp.exp(stats[:, 0] - highest[None, :]), axis=0)
    weights = jnp.exp(scores - highest[None, :])
    potential = jnp.log(column_mass) - highest - jnp.log(column_sum)
    transport = (weights * (N * column_mass / column_sum)[None, :]).astype(jnp.bfloat16)
    return (transport, potential)


def solution(mesh):
    devices = np.asarray(mesh.devices).reshape(2, 2, 4, 2, 2, 2)
    fine = Mesh(devices, AXES)
    in_specs = (P(ROWS, "zh"), P(ROWS, "zh"), P(None, "zh"), P(ROWS), P("zh"), P("zh"))
    out_specs = (P(ROWS, "zh"), P("zh"))
    return jax.shard_map(body, mesh=fine, in_specs=in_specs, out_specs=out_specs, check_vma=False)
```

```python
import jax
import jax.numpy as jnp
import numpy as np
from jax import lax
from jax.sharding import Mesh
from jax.sharding import PartitionSpec as P

N = 32768
AXES = ("yh", "yl", "x", "zl", "core", "zh")
ROWS = ("yh", "yl", "x", "zl", "core")
GATHER = ("yl", "x", "zl", "core")


def body(dist_first, coupling, dist_second, row_potential, column_cost, column_mass):
    zh = lax.axis_index("zh")
    yh = lax.axis_index("yh")
    blocks = coupling.shape[0]
    k_half = coupling.shape[1]
    q_half = dist_second.shape[1]

    message = jnp.concatenate([coupling.reshape(-1), dist_second.reshape(-1)])
    first = lax.ppermute(message, ("yh", "zh"), [(1, 0), (2, 3), (0, 2), (3, 1)])
    second = lax.ppermute(message, ("yh", "zh"), [(1, 2), (2, 1)])
    holds = yh == zh
    split = coupling.size
    mine = coupling
    near = first[:split].reshape(coupling.shape)
    far = second[:split].reshape(coupling.shape)
    piece = jnp.where(holds, jnp.concatenate([mine, near], axis=1), jnp.concatenate([near, far], axis=1))
    second_x = jnp.where(holds, first[split:], second[split:]).reshape(dist_second.shape)

    gathered = lax.all_gather(piece, GATHER, axis=0, tiled=True)

    second_full = jnp.concatenate([dist_second, second_x], axis=1)
    second_k = jnp.concatenate(
        [
            lax.dynamic_slice_in_dim(second_full, zh * k_half, k_half, axis=0),
            lax.dynamic_slice_in_dim(second_full, (1 - zh) * k_half, k_half, axis=0),
        ]
    )

    def partial_gradient(cols):
        product = jnp.dot(
            gathered, second_k[:, cols], preferred_element_type=jnp.float32
        ).astype(jnp.bfloat16)
        return jnp.dot(dist_first, product, preferred_element_type=jnp.float32)

    other_part = partial_gradient(slice(q_half, 2 * q_half))
    arrived = lax.ppermute(other_part, "zh", [(0, 1), (1, 0)])
    own_part = partial_gradient(slice(0, q_half))
    own_part, arrived = lax.optimization_barrier((own_part, arrived))
    gradient = own_part + arrived

    scores = row_potential[:, None] + 2.0 * gradient - column_cost[None, :]
    local_high = jnp.max(scores, axis=0)
    local_sum = jnp.sum(jnp.exp(scores - local_high[None, :]), axis=0)
    pair = jnp.stack([local_high, local_sum])
    row_count = 64
    copies = jnp.broadcast_to(pair, (row_count, *pair.shape))
    pairs = lax.all_to_all(copies, ROWS, 0, 0, tiled=True)
    highest = jnp.max(pairs[:, 0], axis=0)
    column_sum = jnp.sum(pairs[:, 1] * jnp.exp(pairs[:, 0] - highest[None, :]), axis=0)
    weights = jnp.exp(scores - highest[None, :])
    potential = jnp.log(column_mass) - highest - jnp.log(column_sum)
    transport = (weights * (N * column_mass / column_sum)[None, :]).astype(jnp.bfloat16)
    return (transport, potential)


def solution(mesh):
    devices = np.asarray(mesh.devices).reshape(2, 2, 4, 2, 2, 2)
    fine = Mesh(devices, AXES)
    in_specs = (P(ROWS, "zh"), P(ROWS, "zh"), P(None, "zh"), P(ROWS), P("zh"), P("zh"))
    out_specs = (P(ROWS, "zh"), P("zh"))
    return jax.shard_map(body, mesh=fine, in_specs=in_specs, out_specs=out_specs, check_vma=False)
```

```python
import jax
import jax.numpy as jnp
import numpy as np
from jax import lax
from jax.sharding import Mesh
from jax.sharding import PartitionSpec as P

N = 32768
AXES = ("yh", "yl", "x", "zl", "core", "zh")
ROWS = ("yh", "yl", "x", "zl", "core")
GATHER = ("yl", "x", "zl", "core")


def body(dist_first, coupling, dist_second, row_potential, column_cost, column_mass):
    zh = lax.axis_index("zh")
    yh = lax.axis_index("yh")
    blocks = coupling.shape[0]
    k_half = coupling.shape[1]
    q_half = dist_second.shape[1]

    near = lax.ppermute(coupling, ("yh", "zh"), [(1, 0), (2, 3), (0, 2), (3, 1)])
    far = lax.ppermute(coupling, ("yh", "zh"), [(1, 2), (2, 1)])
    holds = yh == zh
    piece = jnp.where(holds, jnp.concatenate([coupling, near], axis=1), jnp.concatenate([near, far], axis=1))
    second_x = lax.ppermute(dist_second, "zh", [(0, 1), (1, 0)])

    gathered = lax.all_gather(piece, GATHER, axis=0, tiled=True)

    second_full = jnp.concatenate([dist_second, second_x], axis=1)
    second_k = jnp.concatenate(
        [
            lax.dynamic_slice_in_dim(second_full, zh * k_half, k_half, axis=0),
            lax.dynamic_slice_in_dim(second_full, (1 - zh) * k_half, k_half, axis=0),
        ]
    )

    product = jnp.dot(gathered, second_k, preferred_element_type=jnp.float32).astype(jnp.bfloat16)
    both = jnp.dot(dist_first, product, preferred_element_type=jnp.float32)
    arrived = lax.ppermute(both[:, q_half:], "zh", [(0, 1), (1, 0)])
    gradient = both[:, :q_half] + arrived

    scores = row_potential[:, None] + 2.0 * gradient - column_cost[None, :]
    local_high = jnp.max(scores, axis=0)
    local_sum = jnp.sum(jnp.exp(scores - local_high[None, :]), axis=0)
    pair = jnp.stack([local_high, local_sum])
    row_count = 64
    copies = jnp.broadcast_to(pair, (row_count, *pair.shape))
    pairs = lax.all_to_all(copies, ROWS, 0, 0, tiled=True)
    highest = jnp.max(pairs[:, 0], axis=0)
    column_sum = jnp.sum(pairs[:, 1] * jnp.exp(pairs[:, 0] - highest[None, :]), axis=0)
    weights = jnp.exp(scores - highest[None, :])
    potential = jnp.log(column_mass) - highest - jnp.log(column_sum)
    transport = (weights * (N * column_mass / column_sum)[None, :]).astype(jnp.bfloat16)
    return (transport, potential)


def solution(mesh):
    devices = np.asarray(mesh.devices).reshape(2, 2, 4, 2, 2, 2)
    fine = Mesh(devices, AXES)
    in_specs = (P(ROWS, "zh"), P(ROWS, "zh"), P(None, "zh"), P(ROWS), P("zh"), P("zh"))
    out_specs = (P(ROWS, "zh"), P("zh"))
    return jax.shard_map(body, mesh=fine, in_specs=in_specs, out_specs=out_specs, check_vma=False)
```

```python
import jax
import jax.numpy as jnp
import numpy as np
from jax import lax
from jax.sharding import Mesh
from jax.sharding import PartitionSpec as P

N = 32768
AXES = ("yh", "yl", "x", "zl", "core", "zh")
ROWS = ("yh", "yl", "x", "zl", "core")
GATHER = ("yl", "x", "zl", "core")


def body(dist_first, coupling, dist_second, row_potential, column_cost, column_mass):
    zh = lax.axis_index("zh")
    yh = lax.axis_index("yh")
    blocks = coupling.shape[0]
    k_half = coupling.shape[1]
    q_half = dist_second.shape[1]

    near = lax.ppermute(coupling, ("yh", "zh"), [(1, 0), (2, 3), (0, 2), (3, 1)])
    far = lax.ppermute(coupling, ("yh", "zh"), [(1, 2), (2, 1)])
    holds = yh == zh
    piece = jnp.where(holds, jnp.concatenate([coupling, near], axis=1), jnp.concatenate([near, far], axis=1))
    second_x = lax.ppermute(dist_second, "zh", [(0, 1), (1, 0)])

    gathered = lax.all_gather(piece, GATHER, axis=0, tiled=True)

    second_full = jnp.concatenate([dist_second, second_x], axis=1)
    second_k = jnp.concatenate(
        [
            lax.dynamic_slice_in_dim(second_full, zh * k_half, k_half, axis=0),
            lax.dynamic_slice_in_dim(second_full, (1 - zh) * k_half, k_half, axis=0),
        ]
    )

    def partial_gradient(cols):
        product = jnp.dot(
            gathered, second_k[:, cols], preferred_element_type=jnp.float32
        ).astype(jnp.bfloat16)
        return jnp.dot(dist_first, product, preferred_element_type=jnp.float32)

    other_part = partial_gradient(slice(q_half, 2 * q_half))
    arrived = lax.ppermute(other_part, "zh", [(0, 1), (1, 0)])
    own_part = partial_gradient(slice(0, q_half))
    own_part, arrived = lax.optimization_barrier((own_part, arrived))
    gradient = own_part + arrived

    scores = row_potential[:, None] + 2.0 * gradient - column_cost[None, :]
    local_high = jnp.max(scores, axis=0)
    local_sum = jnp.sum(jnp.exp(scores - local_high[None, :]), axis=0)
    pair = jnp.stack([local_high, local_sum])
    row_count = 64
    copies = jnp.broadcast_to(pair, (row_count, *pair.shape))
    pairs = lax.all_to_all(copies, ROWS, 0, 0, tiled=True)
    highest = jnp.max(pairs[:, 0], axis=0)
    column_sum = jnp.sum(pairs[:, 1] * jnp.exp(pairs[:, 0] - highest[None, :]), axis=0)
    weights = jnp.exp(scores - highest[None, :])
    potential = jnp.log(column_mass) - highest - jnp.log(column_sum)
    transport = (weights * (N * column_mass / column_sum)[None, :]).astype(jnp.bfloat16)
    return (transport, potential)


def solution(mesh):
    devices = np.asarray(mesh.devices).reshape(2, 2, 4, 2, 2, 2)
    fine = Mesh(devices, AXES)
    in_specs = (P(ROWS, "zh"), P(ROWS, "zh"), P(None, "zh"), P(ROWS), P("zh"), P("zh"))
    out_specs = (P(ROWS, "zh"), P("zh"))
    return jax.shard_map(body, mesh=fine, in_specs=in_specs, out_specs=out_specs, check_vma=False)
```

```python
import jax
import jax.numpy as jnp
import numpy as np
from jax import lax
from jax.experimental import pallas as pl
from jax.experimental.pallas import tpu as pltpu
from jax.sharding import Mesh
from jax.sharding import PartitionSpec as P

N = 32768
AXES = ("yh", "yl", "x", "zl", "core", "zh")
ROWS = ("yh", "yl", "x", "zl", "core")
GATHER = ("yl", "x", "zl", "core")


def _panel_kernel(d_ref, c_ref, s_ref, o_ref):
    @pl.when(pl.program_id(0) == 0)
    def _():
        o_ref[...] = jnp.zeros_like(o_ref)
    product = jnp.dot(c_ref[...], s_ref[...], preferred_element_type=jnp.float32).astype(jnp.bfloat16)
    o_ref[...] += jnp.dot(d_ref[...], product, preferred_element_type=jnp.float32)

def panel_gradient(dist_first, coupling_rows, second_cols, step=2048):
    rows, inner = dist_first.shape
    k = coupling_rows.shape[1]
    q = second_cols.shape[1]
    flops = 2 * inner * k * q + 2 * rows * inner * q
    bytes_accessed = 2 * (dist_first.size + coupling_rows.size + second_cols.size) + 4 * rows * q
    return pl.pallas_call(
        _panel_kernel,
        out_shape=jax.ShapeDtypeStruct((rows, q), jnp.float32),
        grid=(inner // step,),
        in_specs=[
            pl.BlockSpec((rows, step), lambda j: (0, j)),
            pl.BlockSpec((step, k), lambda j: (j, 0)),
            pl.BlockSpec((k, q), lambda j: (0, 0)),
        ],
        out_specs=pl.BlockSpec((rows, q), lambda j: (0, 0)),
        compiler_params=pltpu.CompilerParams(dimension_semantics=("arbitrary",)),
        cost_estimate=pl.CostEstimate(flops=flops, transcendentals=0, bytes_accessed=bytes_accessed),
    )(dist_first, coupling_rows, second_cols)


def body(dist_first, coupling, dist_second, row_potential, column_cost, column_mass):
    zh = lax.axis_index("zh")
    yh = lax.axis_index("yh")
    blocks = coupling.shape[0]
    k_half = coupling.shape[1]
    q_half = dist_second.shape[1]

    near = lax.ppermute(coupling, ("yh", "zh"), [(1, 0), (2, 3), (0, 2), (3, 1)])
    far = lax.ppermute(coupling, ("yh", "zh"), [(1, 2), (2, 1)])
    holds = yh == zh
    piece = jnp.where(holds, jnp.concatenate([coupling, near], axis=1), jnp.concatenate([near, far], axis=1))
    second_x = lax.ppermute(dist_second, "zh", [(0, 1), (1, 0)])

    gathered = lax.all_gather(piece, GATHER, axis=0, tiled=True)

    second_full = jnp.concatenate([dist_second, second_x], axis=1)
    second_k = jnp.concatenate(
        [
            lax.dynamic_slice_in_dim(second_full, zh * k_half, k_half, axis=0),
            lax.dynamic_slice_in_dim(second_full, (1 - zh) * k_half, k_half, axis=0),
        ]
    )

    def partial_gradient(cols):
        return panel_gradient(dist_first, gathered, second_k[:, cols])

    other_part = partial_gradient(slice(q_half, 2 * q_half))
    arrived = lax.ppermute(other_part, "zh", [(0, 1), (1, 0)])
    own_part = partial_gradient(slice(0, q_half))
    own_part, arrived = lax.optimization_barrier((own_part, arrived))
    gradient = own_part + arrived

    scores = row_potential[:, None] + 2.0 * gradient - column_cost[None, :]
    local_high = jnp.max(scores, axis=0)
    local_sum = jnp.sum(jnp.exp(scores - local_high[None, :]), axis=0)
    pair = jnp.stack([local_high, local_sum])
    row_count = 64
    copies = jnp.broadcast_to(pair, (row_count, *pair.shape))
    pairs = lax.all_to_all(copies, ROWS, 0, 0, tiled=True)
    highest = jnp.max(pairs[:, 0], axis=0)
    column_sum = jnp.sum(pairs[:, 1] * jnp.exp(pairs[:, 0] - highest[None, :]), axis=0)
    weights = jnp.exp(scores - highest[None, :])
    potential = jnp.log(column_mass) - highest - jnp.log(column_sum)
    transport = (weights * (N * column_mass / column_sum)[None, :]).astype(jnp.bfloat16)
    return (transport, potential)


def solution(mesh):
    devices = np.asarray(mesh.devices).reshape(2, 2, 4, 2, 2, 2)
    fine = Mesh(devices, AXES)
    in_specs = (P(ROWS, "zh"), P(ROWS, "zh"), P(None, "zh"), P(ROWS), P("zh"), P("zh"))
    out_specs = (P(ROWS, "zh"), P("zh"))
    return jax.shard_map(body, mesh=fine, in_specs=in_specs, out_specs=out_specs, check_vma=False)
```

```python
import jax
import jax.numpy as jnp
import numpy as np
from jax import lax
from jax.sharding import Mesh
from jax.sharding import PartitionSpec as P

N = 32768
AXES = ("yh", "yl", "x", "zl", "core", "zh")
ROWS = ("yh", "yl", "x", "zl", "core")
GATHER = ("yl", "x", "zl", "core")


def body(dist_first, coupling, dist_second, row_potential, column_cost, column_mass):
    zh = lax.axis_index("zh")
    yh = lax.axis_index("yh")
    blocks = coupling.shape[0]
    k_half = coupling.shape[1]
    q_half = dist_second.shape[1]

    near = lax.ppermute(coupling, ("yh", "zh"), [(1, 0), (2, 3), (0, 2), (3, 1)])
    far = lax.ppermute(coupling, ("yh", "zh"), [(1, 2), (2, 1)])
    holds = yh == zh
    piece = jnp.where(holds, jnp.concatenate([coupling, near], axis=1), jnp.concatenate([near, far], axis=1))
    second_x = lax.ppermute(dist_second, "zh", [(0, 1), (1, 0)])
    piece, second_x = lax.optimization_barrier((piece, second_x))

    gathered = lax.all_gather(piece, GATHER, axis=0, tiled=True)

    second_full = jnp.concatenate([dist_second, second_x], axis=1)
    second_k = jnp.concatenate(
        [
            lax.dynamic_slice_in_dim(second_full, zh * k_half, k_half, axis=0),
            lax.dynamic_slice_in_dim(second_full, (1 - zh) * k_half, k_half, axis=0),
        ]
    )

    def partial_gradient(cols):
        product = jnp.dot(
            gathered, second_k[:, cols], preferred_element_type=jnp.float32
        ).astype(jnp.bfloat16)
        return jnp.dot(dist_first, product, preferred_element_type=jnp.float32)

    other_part = partial_gradient(slice(q_half, 2 * q_half))
    arrived = lax.ppermute(other_part, "zh", [(0, 1), (1, 0)])
    own_part = partial_gradient(slice(0, q_half))
    own_part, arrived = lax.optimization_barrier((own_part, arrived))
    gradient = own_part + arrived

    scores = row_potential[:, None] + 2.0 * gradient - column_cost[None, :]
    local_high = jnp.max(scores, axis=0)
    local_sum = jnp.sum(jnp.exp(scores - local_high[None, :]), axis=0)
    pair = jnp.stack([local_high, local_sum])
    row_count = 64
    copies = jnp.broadcast_to(pair, (row_count, *pair.shape))
    pairs = lax.all_to_all(copies, ROWS, 0, 0, tiled=True)
    highest = jnp.max(pairs[:, 0], axis=0)
    column_sum = jnp.sum(pairs[:, 1] * jnp.exp(pairs[:, 0] - highest[None, :]), axis=0)
    weights = jnp.exp(scores - highest[None, :])
    potential = jnp.log(column_mass) - highest - jnp.log(column_sum)
    transport = (weights * (N * column_mass / column_sum)[None, :]).astype(jnp.bfloat16)
    return (transport, potential)


def solution(mesh):
    devices = np.asarray(mesh.devices).reshape(2, 2, 4, 2, 2, 2)
    fine = Mesh(devices, AXES)
    in_specs = (P(ROWS, "zh"), P(ROWS, "zh"), P(None, "zh"), P(ROWS), P("zh"), P("zh"))
    out_specs = (P(ROWS, "zh"), P("zh"))
    return jax.shard_map(body, mesh=fine, in_specs=in_specs, out_specs=out_specs, check_vma=False)
```

```python
import jax
import jax.numpy as jnp
import numpy as np
from jax import lax
from jax.sharding import Mesh
from jax.sharding import PartitionSpec as P

N = 32768
AXES = ("yh", "yl", "x", "zl", "core", "zh")
ROWS = ("yh", "yl", "x", "zl", "core")


def body(dist_first, coupling, dist_second, row_potential, column_cost, column_mass):
    zh = lax.axis_index("zh")
    yh = lax.axis_index("yh")
    blocks = coupling.shape[0]
    k_half = coupling.shape[1]
    q_half = dist_second.shape[1]

    near = lax.ppermute(coupling, ("yh", "zh"), [(1, 0), (2, 3), (0, 2), (3, 1)])
    far = lax.ppermute(coupling, ("yh", "zh"), [(1, 2), (2, 1)])
    holds = yh == zh
    piece = jnp.where(holds, jnp.concatenate([coupling, near], axis=1), jnp.concatenate([near, far], axis=1))
    second_x = lax.ppermute(dist_second, "zh", [(0, 1), (1, 0)])

    pair_rows = lax.all_gather(piece, "yl", axis=0, tiled=True)
    gathered = lax.all_gather(pair_rows, ("x", "zl", "core"), axis=0, tiled=True)
    gathered = gathered.reshape(4, 2, 2, 2, blocks, 2 * k_half)
    gathered = jnp.transpose(gathered, (3, 0, 1, 2, 4, 5)).reshape(-1, 2 * k_half)

    second_full = jnp.concatenate([dist_second, second_x], axis=1)
    second_k = jnp.concatenate(
        [
            lax.dynamic_slice_in_dim(second_full, zh * k_half, k_half, axis=0),
            lax.dynamic_slice_in_dim(second_full, (1 - zh) * k_half, k_half, axis=0),
        ]
    )

    def partial_gradient(cols):
        product = jnp.dot(
            gathered, second_k[:, cols], preferred_element_type=jnp.float32
        ).astype(jnp.bfloat16)
        return jnp.dot(dist_first, product, preferred_element_type=jnp.float32)

    other_part = partial_gradient(slice(q_half, 2 * q_half))
    arrived = lax.ppermute(other_part, "zh", [(0, 1), (1, 0)])
    own_part = partial_gradient(slice(0, q_half))
    own_part, arrived = lax.optimization_barrier((own_part, arrived))
    gradient = own_part + arrived

    scores = row_potential[:, None] + 2.0 * gradient - column_cost[None, :]
    local_high = jnp.max(scores, axis=0)
    local_sum = jnp.sum(jnp.exp(scores - local_high[None, :]), axis=0)
    pair = jnp.stack([local_high, local_sum])
    row_count = 64
    copies = jnp.broadcast_to(pair, (row_count, *pair.shape))
    pairs = lax.all_to_all(copies, ROWS, 0, 0, tiled=True)
    highest = jnp.max(pairs[:, 0], axis=0)
    column_sum = jnp.sum(pairs[:, 1] * jnp.exp(pairs[:, 0] - highest[None, :]), axis=0)
    weights = jnp.exp(scores - highest[None, :])
    potential = jnp.log(column_mass) - highest - jnp.log(column_sum)
    transport = (weights * (N * column_mass / column_sum)[None, :]).astype(jnp.bfloat16)
    return (transport, potential)


def solution(mesh):
    devices = np.asarray(mesh.devices).reshape(2, 2, 4, 2, 2, 2)
    fine = Mesh(devices, AXES)
    in_specs = (P(ROWS, "zh"), P(ROWS, "zh"), P(None, "zh"), P(ROWS), P("zh"), P("zh"))
    out_specs = (P(ROWS, "zh"), P("zh"))
    return jax.shard_map(body, mesh=fine, in_specs=in_specs, out_specs=out_specs, check_vma=False)
```

```python
import jax
import jax.numpy as jnp
import numpy as np
from jax import lax
from jax.sharding import Mesh
from jax.sharding import PartitionSpec as P

N = 32768
AXES = ("yh", "yl", "x", "zl", "core", "zh")
ROWS = ("yh", "yl", "x", "zl", "core")


def body(dist_first, coupling, dist_second, row_potential, column_cost, column_mass):
    zh = lax.axis_index("zh")
    yh = lax.axis_index("yh")
    blocks = coupling.shape[0]
    k_half = coupling.shape[1]
    q_half = dist_second.shape[1]

    near = lax.ppermute(coupling, ("yh", "zh"), [(1, 0), (2, 3), (0, 2), (3, 1)])
    far = lax.ppermute(coupling, ("yh", "zh"), [(1, 2), (2, 1)])
    def at(a, b, c):
        return a * 4 + b * 2 + c

    first_pairs, second_pairs = [], []
    for a in range(2):
        for b in range(2):
            first_pairs += [(at(a, b, a), at(a, 1 - b, a)), (at(a, b, 1 - a), at(1 - a, 1 - b, a))]
            second_pairs += [(at(a, b, a), at(1 - a, 1 - b, a)), (at(a, b, 1 - a), at(a, 1 - b, a))]
    other_first = lax.ppermute(coupling, ("yh", "yl", "zh"), first_pairs)
    other_second = lax.ppermute(coupling, ("yh", "yl", "zh"), second_pairs)
    holds = yh == zh
    own_block = jnp.where(holds, jnp.concatenate([coupling, near], axis=1), jnp.concatenate([near, far], axis=1))
    other_block = jnp.where(
        holds,
        jnp.concatenate([other_first, other_second], axis=1),
        jnp.concatenate([other_second, other_first], axis=1),
    )
    yl = lax.axis_index("yl")
    piece = jnp.where(
        yl == 0,
        jnp.concatenate([own_block, other_block], axis=0),
        jnp.concatenate([other_block, own_block], axis=0),
    )
    second_x = lax.ppermute(dist_second, "zh", [(0, 1), (1, 0)])

    gathered = lax.all_gather(piece, ("x", "zl", "core"), axis=0, tiled=True)
    gathered = gathered.reshape(4, 2, 2, 2, blocks, 2 * k_half)
    gathered = jnp.transpose(gathered, (3, 0, 1, 2, 4, 5)).reshape(-1, 2 * k_half)

    second_full = jnp.concatenate([dist_second, second_x], axis=1)
    second_k = jnp.concatenate(
        [
            lax.dynamic_slice_in_dim(second_full, zh * k_half, k_half, axis=0),
            lax.dynamic_slice_in_dim(second_full, (1 - zh) * k_half, k_half, axis=0),
        ]
    )

    def partial_gradient(cols):
        product = jnp.dot(
            gathered, second_k[:, cols], preferred_element_type=jnp.float32
        ).astype(jnp.bfloat16)
        return jnp.dot(dist_first, product, preferred_element_type=jnp.float32)

    other_part = partial_gradient(slice(q_half, 2 * q_half))
    arrived = lax.ppermute(other_part, "zh", [(0, 1), (1, 0)])
    own_part = partial_gradient(slice(0, q_half))
    own_part, arrived = lax.optimization_barrier((own_part, arrived))
    gradient = own_part + arrived

    scores = row_potential[:, None] + 2.0 * gradient - column_cost[None, :]
    local_high = jnp.max(scores, axis=0)
    local_sum = jnp.sum(jnp.exp(scores - local_high[None, :]), axis=0)
    pair = jnp.stack([local_high, local_sum])
    row_count = 64
    copies = jnp.broadcast_to(pair, (row_count, *pair.shape))
    pairs = lax.all_to_all(copies, ROWS, 0, 0, tiled=True)
    highest = jnp.max(pairs[:, 0], axis=0)
    column_sum = jnp.sum(pairs[:, 1] * jnp.exp(pairs[:, 0] - highest[None, :]), axis=0)
    weights = jnp.exp(scores - highest[None, :])
    potential = jnp.log(column_mass) - highest - jnp.log(column_sum)
    transport = (weights * (N * column_mass / column_sum)[None, :]).astype(jnp.bfloat16)
    return (transport, potential)


def solution(mesh):
    devices = np.asarray(mesh.devices).reshape(2, 2, 4, 2, 2, 2)
    fine = Mesh(devices, AXES)
    in_specs = (P(ROWS, "zh"), P(ROWS, "zh"), P(None, "zh"), P(ROWS), P("zh"), P("zh"))
    out_specs = (P(ROWS, "zh"), P("zh"))
    return jax.shard_map(body, mesh=fine, in_specs=in_specs, out_specs=out_specs, check_vma=False)
```

```python
import jax
import jax.numpy as jnp
import numpy as np
from jax import lax
from jax.sharding import Mesh
from jax.sharding import PartitionSpec as P

N = 32768
AXES = ("yh", "yl", "x", "zl", "core", "zh")
ROWS = ("yh", "yl", "x", "zl", "core")


def body(dist_first, coupling, dist_second, row_potential, column_cost, column_mass):
    zh = lax.axis_index("zh")
    yh = lax.axis_index("yh")
    blocks = coupling.shape[0]
    k_half = coupling.shape[1]
    q_half = dist_second.shape[1]

    near = lax.ppermute(coupling, ("yh", "zh"), [(1, 0), (2, 3), (0, 2), (3, 1)])
    far = lax.ppermute(coupling, ("yh", "zh"), [(1, 2), (2, 1)])
    def at(a, b, c):
        return a * 4 + b * 2 + c

    first_pairs, second_pairs = [], []
    for a in range(2):
        for b in range(2):
            first_pairs += [(at(a, b, a), at(a, 1 - b, a)), (at(a, b, 1 - a), at(1 - a, 1 - b, a))]
            second_pairs += [(at(a, b, a), at(1 - a, 1 - b, a)), (at(a, b, 1 - a), at(a, 1 - b, a))]
    other_first = lax.ppermute(coupling, ("yh", "yl", "zh"), first_pairs)
    other_second = lax.ppermute(coupling, ("yh", "yl", "zh"), second_pairs)
    holds = yh == zh
    own_block = jnp.where(holds, jnp.concatenate([coupling, near], axis=1), jnp.concatenate([near, far], axis=1))
    other_block = jnp.where(
        holds,
        jnp.concatenate([other_first, other_second], axis=1),
        jnp.concatenate([other_second, other_first], axis=1),
    )
    yl = lax.axis_index("yl")
    piece = jnp.where(yl == 0, jnp.stack([own_block, other_block]), jnp.stack([other_block, own_block]))
    second_x = lax.ppermute(dist_second, "zh", [(0, 1), (1, 0)])

    gathered = lax.all_gather(piece, ("x", "zl", "core"), axis=1, tiled=True).reshape(-1, 2 * k_half)

    second_full = jnp.concatenate([dist_second, second_x], axis=1)
    second_k = jnp.concatenate(
        [
            lax.dynamic_slice_in_dim(second_full, zh * k_half, k_half, axis=0),
            lax.dynamic_slice_in_dim(second_full, (1 - zh) * k_half, k_half, axis=0),
        ]
    )

    def partial_gradient(cols):
        product = jnp.dot(
            gathered, second_k[:, cols], preferred_element_type=jnp.float32
        ).astype(jnp.bfloat16)
        return jnp.dot(dist_first, product, preferred_element_type=jnp.float32)

    other_part = partial_gradient(slice(q_half, 2 * q_half))
    arrived = lax.ppermute(other_part, "zh", [(0, 1), (1, 0)])
    own_part = partial_gradient(slice(0, q_half))
    own_part, arrived = lax.optimization_barrier((own_part, arrived))
    gradient = own_part + arrived

    scores = row_potential[:, None] + 2.0 * gradient - column_cost[None, :]
    local_high = jnp.max(scores, axis=0)
    local_sum = jnp.sum(jnp.exp(scores - local_high[None, :]), axis=0)
    pair = jnp.stack([local_high, local_sum])
    row_count = 64
    copies = jnp.broadcast_to(pair, (row_count, *pair.shape))
    pairs = lax.all_to_all(copies, ROWS, 0, 0, tiled=True)
    highest = jnp.max(pairs[:, 0], axis=0)
    column_sum = jnp.sum(pairs[:, 1] * jnp.exp(pairs[:, 0] - highest[None, :]), axis=0)
    weights = jnp.exp(scores - highest[None, :])
    potential = jnp.log(column_mass) - highest - jnp.log(column_sum)
    transport = (weights * (N * column_mass / column_sum)[None, :]).astype(jnp.bfloat16)
    return (transport, potential)


def solution(mesh):
    devices = np.asarray(mesh.devices).reshape(2, 2, 4, 2, 2, 2)
    fine = Mesh(devices, AXES)
    in_specs = (P(ROWS, "zh"), P(ROWS, "zh"), P(None, "zh"), P(ROWS), P("zh"), P("zh"))
    out_specs = (P(ROWS, "zh"), P("zh"))
    return jax.shard_map(body, mesh=fine, in_specs=in_specs, out_specs=out_specs, check_vma=False)
```

```python
import jax
import jax.numpy as jnp
import numpy as np
from jax import lax
from jax.sharding import Mesh
from jax.sharding import PartitionSpec as P

N = 32768
AXES = ("yh", "yl", "x", "zl", "core", "zh")
ROWS = ("yh", "yl", "x", "zl", "core")


def body(dist_first, coupling, dist_second, row_potential, column_cost, column_mass):
    zh = lax.axis_index("zh")
    yh = lax.axis_index("yh")
    blocks = coupling.shape[0]
    k_half = coupling.shape[1]
    q_half = dist_second.shape[1]

    column = lax.axis_size("yh") * lax.axis_size("yl") * lax.axis_size("zh")
    copies = jnp.broadcast_to(coupling, (column, *coupling.shape))
    column_blocks = lax.all_to_all(copies, ("yh", "yl", "zh"), 0, 0, tiled=True)
    column_blocks = column_blocks.reshape(2, 2, 2, blocks, k_half)
    mine = lax.dynamic_index_in_dim(column_blocks, zh, axis=0, keepdims=False)
    piece = jnp.concatenate(
        [
            lax.dynamic_index_in_dim(mine, zh, axis=1, keepdims=False),
            lax.dynamic_index_in_dim(mine, 1 - zh, axis=1, keepdims=False),
        ],
        axis=2,
    )
    second_x = lax.ppermute(dist_second, "zh", [(0, 1), (1, 0)])

    gathered = lax.all_gather(piece, ("x", "zl", "core"), axis=1, tiled=True).reshape(-1, 2 * k_half)

    second_full = jnp.concatenate([dist_second, second_x], axis=1)
    second_k = jnp.concatenate(
        [
            lax.dynamic_slice_in_dim(second_full, zh * k_half, k_half, axis=0),
            lax.dynamic_slice_in_dim(second_full, (1 - zh) * k_half, k_half, axis=0),
        ]
    )

    def partial_gradient(cols):
        product = jnp.dot(
            gathered, second_k[:, cols], preferred_element_type=jnp.float32
        ).astype(jnp.bfloat16)
        return jnp.dot(dist_first, product, preferred_element_type=jnp.float32)

    other_part = partial_gradient(slice(q_half, 2 * q_half))
    arrived = lax.ppermute(other_part, "zh", [(0, 1), (1, 0)])
    own_part = partial_gradient(slice(0, q_half))
    own_part, arrived = lax.optimization_barrier((own_part, arrived))
    gradient = own_part + arrived

    scores = row_potential[:, None] + 2.0 * gradient - column_cost[None, :]
    local_high = jnp.max(scores, axis=0)
    local_sum = jnp.sum(jnp.exp(scores - local_high[None, :]), axis=0)
    pair = jnp.stack([local_high, local_sum])
    row_count = 64
    copies = jnp.broadcast_to(pair, (row_count, *pair.shape))
    pairs = lax.all_to_all(copies, ROWS, 0, 0, tiled=True)
    highest = jnp.max(pairs[:, 0], axis=0)
    column_sum = jnp.sum(pairs[:, 1] * jnp.exp(pairs[:, 0] - highest[None, :]), axis=0)
    weights = jnp.exp(scores - highest[None, :])
    potential = jnp.log(column_mass) - highest - jnp.log(column_sum)
    transport = (weights * (N * column_mass / column_sum)[None, :]).astype(jnp.bfloat16)
    return (transport, potential)


def solution(mesh):
    devices = np.asarray(mesh.devices).reshape(2, 2, 4, 2, 2, 2)
    fine = Mesh(devices, AXES)
    in_specs = (P(ROWS, "zh"), P(ROWS, "zh"), P(None, "zh"), P(ROWS), P("zh"), P("zh"))
    out_specs = (P(ROWS, "zh"), P("zh"))
    return jax.shard_map(body, mesh=fine, in_specs=in_specs, out_specs=out_specs, check_vma=False)
```

```python
import jax
import jax.numpy as jnp
import numpy as np
from jax import lax
from jax.experimental.layout import Layout, with_layout_constraint
from jax.sharding import Mesh
from jax.sharding import PartitionSpec as P

N = 32768
AXES = ("yh", "yl", "x", "zl", "core", "zh")
ROWS = ("yh", "yl", "x", "zl", "core")


def body(dist_first, coupling, dist_second, row_potential, column_cost, column_mass):
    zh = lax.axis_index("zh")
    yh = lax.axis_index("yh")
    blocks = coupling.shape[0]
    k_half = coupling.shape[1]
    q_half = dist_second.shape[1]

    near = lax.ppermute(coupling, ("yh", "zh"), [(1, 0), (2, 3), (0, 2), (3, 1)])
    far = lax.ppermute(coupling, ("yh", "zh"), [(1, 2), (2, 1)])
    def at(a, b, c):
        return a * 4 + b * 2 + c

    first_pairs, second_pairs = [], []
    for a in range(2):
        for b in range(2):
            first_pairs += [(at(a, b, a), at(a, 1 - b, a)), (at(a, b, 1 - a), at(1 - a, 1 - b, a))]
            second_pairs += [(at(a, b, a), at(1 - a, 1 - b, a)), (at(a, b, 1 - a), at(a, 1 - b, a))]
    other_first = lax.ppermute(coupling, ("yh", "yl", "zh"), first_pairs)
    other_second = lax.ppermute(coupling, ("yh", "yl", "zh"), second_pairs)
    holds = yh == zh
    own_block = jnp.where(holds, jnp.concatenate([coupling, near], axis=1), jnp.concatenate([near, far], axis=1))
    other_block = jnp.where(
        holds,
        jnp.concatenate([other_first, other_second], axis=1),
        jnp.concatenate([other_second, other_first], axis=1),
    )
    yl = lax.axis_index("yl")
    piece = jnp.where(yl == 0, jnp.stack([own_block, other_block]), jnp.stack([other_block, own_block]))
    second_x = lax.ppermute(dist_second, "zh", [(0, 1), (1, 0)])

    gathered = lax.all_gather(piece, ("x", "zl", "core"), axis=1, tiled=True).reshape(-1, 2 * k_half)

    second_full = jnp.concatenate([dist_second, second_x], axis=1)
    second_k = jnp.concatenate(
        [
            lax.dynamic_slice_in_dim(second_full, zh * k_half, k_half, axis=0),
            lax.dynamic_slice_in_dim(second_full, (1 - zh) * k_half, k_half, axis=0),
        ]
    )

    def partial_gradient(cols):
        product = jnp.dot(
            gathered, second_k[:, cols], preferred_element_type=jnp.float32
        ).astype(jnp.bfloat16)
        part = jnp.dot(dist_first, product, preferred_element_type=jnp.float32)
        return with_layout_constraint(part, Layout((0, 1)))

    other_part = partial_gradient(slice(q_half, 2 * q_half))
    arrived = lax.ppermute(other_part, "zh", [(0, 1), (1, 0)])
    own_part = partial_gradient(slice(0, q_half))
    own_part, arrived = lax.optimization_barrier((own_part, arrived))
    gradient = own_part + arrived

    scores = row_potential[:, None] + 2.0 * gradient - column_cost[None, :]
    local_high = jnp.max(scores, axis=0)
    local_sum = jnp.sum(jnp.exp(scores - local_high[None, :]), axis=0)
    pair = jnp.stack([local_high, local_sum])
    row_count = 64
    copies = jnp.broadcast_to(pair, (row_count, *pair.shape))
    pairs = lax.all_to_all(copies, ROWS, 0, 0, tiled=True)
    highest = jnp.max(pairs[:, 0], axis=0)
    column_sum = jnp.sum(pairs[:, 1] * jnp.exp(pairs[:, 0] - highest[None, :]), axis=0)
    weights = jnp.exp(scores - highest[None, :])
    potential = jnp.log(column_mass) - highest - jnp.log(column_sum)
    transport = (weights * (N * column_mass / column_sum)[None, :]).astype(jnp.bfloat16)
    return (transport, potential)


def solution(mesh):
    devices = np.asarray(mesh.devices).reshape(2, 2, 4, 2, 2, 2)
    fine = Mesh(devices, AXES)
    in_specs = (P(ROWS, "zh"), P(ROWS, "zh"), P(None, "zh"), P(ROWS), P("zh"), P("zh"))
    out_specs = (P(ROWS, "zh"), P("zh"))
    return jax.shard_map(body, mesh=fine, in_specs=in_specs, out_specs=out_specs, check_vma=False)
```
